256 devices in a mesh: row: 16 (over x, y_hi, core), col: 16 (over y_lo, z).
Axes of the slice: x: 4, y: 4 (y_hi: 2, y_lo: 2; y = y_hi * 2 + y_lo), z: 8, core: 2. Of those that a mesh axis runs over, the one named last changes fastest.
Arguments:
- left_rows: float32 [1024, 61440], P('col', 'row'), may hold values from -1.2 to 1.2
- right_cols: float32 [61440, 4096], P('col', 'row'), may hold values from -1.2 to 1.2
- left_pattern: int32 [16, 240], replicated, may hold values from 0 to 1, as said below
- right_pattern: int32 [240, 16], replicated, may hold values from 0 to 1, as said below
Outputs:
- square_terms: float32 [1024, 4096], P('col', 'row')
The draws below stay inside these ranges and needn't reach their ends.
Inputs may be any that keep to these rules, and one draw needn't show every extreme that they name: Every device's tile of left_pattern (row b, inner blocks from a * 15) has between 1 and 3 occupied blocks, and some tile has exactly 3 in every draw. Every device's tile of right_pattern (inner blocks from b * 15, column a) has between 1 and 3 occupied blocks, and some tile has exactly 3 in every draw.
All inputs are finite; a program needn't handle non-finite values.
Results may differ from the reference program's by a relative error of at most 0.0001.
Values sent between devices are 32-bit elements; how exact they have to be, the bound alone decides.
No kernel may reach another device: no remote copies, remote signals or barrier semaphores. Data moves between devices by JAX's collectives and lax.ppermute only.
A program may use at most 128 MiB of HBM per device.

```python
import jax
import jax.numpy as jnp
from jax import lax

BLK = 256
NBLK = 240
LROWS = 64
STEPS = 4
BPD = 15
TROWS = 15
LCAP = 3
RCAP = 3
ORDER = 61440
WROWS = 1024
WCOLS = 4096
N_ROW = 16
N_COL = 16


def occupied_tiles(key, tile_count, tile_blocks, most):
    extra_key = jax.random.fold_in(key, 1)
    busy_key = jax.random.fold_in(key, 2)
    pick_key = jax.random.fold_in(key, 3)
    order_key = jax.random.fold_in(key, 4)
    extra = jax.random.randint(extra_key, (tile_count,), 2, most + 1)
    busy = jax.random.randint(busy_key, (tile_count,), 0, 4) == 0
    counts = jnp.where(busy, extra, 1)
    chosen = jax.random.randint(pick_key, (), 0, tile_count)
    counts = jnp.where(jnp.arange(tile_count) == chosen, most, counts)
    permuted = jax.vmap(lambda subkey: jax.random.permutation(subkey, tile_blocks))(jax.random.split(order_key, tile_count))
    ranked = jnp.argsort(permuted, axis=1)
    return (ranked < counts[:, None]).astype(jnp.int32)


def draw_left_pattern(key, part):
    occupied = occupied_tiles(jax.random.fold_in(key, 17), N_COL * N_ROW, BPD, LCAP)
    return occupied.reshape(N_COL, N_ROW * BPD)


def draw_right_pattern(key, part):
    occupied = occupied_tiles(jax.random.fold_in(key, 29), N_COL * N_ROW, TROWS, RCAP)
    return occupied.reshape(N_COL, N_ROW, TROWS).transpose(0, 2, 1).reshape(N_COL * TROWS, N_ROW)


def levels(rng, dims, pieces, least, high):
    def one(axis_at, parts):
        draws = jax.random.uniform(jax.random.fold_in(jax.random.fold_in(rng, 6), axis_at), (parts,), jnp.float32, least / len(pieces), high / len(pieces))
        return jnp.repeat(jnp.exp(draws), dims[axis_at] // parts).reshape((-1,) + (1,) * (len(dims) - axis_at - 1))

    factor_of = one(*pieces[0])
    for cut in pieces[1:]:
        factor_of = factor_of * one(*cut)
    return factor_of


def normal_values(own_key, shape, deviation, reach, cuts=(), held_as=jnp.bfloat16):
    result = deviation * jax.random.normal(own_key, shape, jnp.float32)
    if cuts:
        result = result * levels(own_key, shape, cuts, -0.22, 0.18)
    return jnp.clip(result, -reach, reach).astype(held_as)


def setup_inputs(seed: int = 0) -> dict:
    seeds = jax.random.split(jax.random.key(seed), 5)
    return {
        "left_rows": normal_values(seeds[0], (WROWS, ORDER), 0.2, 1.2, ((0, 16), (1, 16)), jnp.float32),
        "right_cols": normal_values(seeds[1], (ORDER, WCOLS), 0.2, 1.2, ((0, 16), (1, 16)), jnp.float32),
        "left_pattern": draw_left_pattern(jax.random.fold_in(seeds[4], 71), 0),
        "right_pattern": draw_right_pattern(jax.random.fold_in(seeds[4], 71), 0),
    }


def reference(left_rows, right_cols, left_pattern, right_pattern):
    left_mask = left_pattern.astype(jnp.float32)
    right_mask = right_pattern.astype(jnp.float32)
    left_masked = (left_rows.reshape(N_COL, LROWS, NBLK, BLK) * left_mask[:, None, :, None]).reshape(N_COL * LROWS, NBLK * BLK)
    right_masked = (right_cols.reshape(NBLK, BLK, N_ROW, BLK) * right_mask[:, None, :, None]).reshape(NBLK * BLK, N_ROW * BLK)
    ratio = N_ROW // N_COL
    inner = BPD * BLK
    panels = []
    for column in range(N_COL):
        total = jnp.zeros((LROWS, N_ROW * BLK), jnp.float32)
        for step in range(STEPS):
            inner_panel = (column * ratio + step) % N_ROW
            left = left_masked[column * LROWS:(column + 1) * LROWS, inner_panel * inner:(inner_panel + 1) * inner]
            right = right_masked[inner_panel * inner:(inner_panel + 1) * inner, :]
            total = total + jnp.dot(left, right, precision=lax.Precision.HIGHEST, preferred_element_type=jnp.float32)
        panels.append(total)
    return jnp.concatenate(panels, axis=0)
```

```python
import jax
import jax.numpy as jnp
from jax import lax
from jax.sharding import PartitionSpec as P

STEPS = 4
CAP = 3


def from_behind(value, axis, steps):
    count = lax.axis_size(axis)
    pairs = [(source, (source - steps) % count) for source in range(count)]
    return lax.ppermute(value, axis, pairs)


def occupied(flags, cap):
    flags = flags != 0
    rank = jnp.cumsum(flags.astype(jnp.int32)) - 1
    where = jnp.arange(flags.shape[0], dtype=jnp.int32)
    hit = flags[None, :] & (rank[None, :] == jnp.arange(cap, dtype=jnp.int32)[:, None])
    index = jnp.sum(jnp.where(hit, where[None, :], 0), axis=1)
    return index, jnp.any(hit, axis=1)


def left_flags(left_pattern, block_row, block_col, per_k):
    return lax.dynamic_slice(left_pattern, (block_row, block_col * per_k), (1, per_k)).reshape(-1)


def right_flags(right_pattern, block_row, block_col, trows):
    return lax.dynamic_slice(right_pattern, (block_row * trows, block_col), (trows, 1)).reshape(-1)


def pick_cols(x, index, blk):
    return jnp.concatenate(
        [lax.dynamic_slice_in_dim(x, index[s] * blk, blk, axis=1) for s in range(index.shape[0])], axis=1
    )


def pick_rows(x, index, blk):
    return jnp.concatenate(
        [lax.dynamic_slice_in_dim(x, index[s] * blk, blk, axis=0) for s in range(index.shape[0])], axis=0
    )


def body(left_rows, right_cols, left_pattern, right_pattern):
    nrow = lax.axis_size("row")
    ncol = lax.axis_size("col")
    ratio = nrow // ncol
    lrows, left_width = left_rows.shape
    right_height, blk = right_cols.shape
    per_k = left_width // blk
    trows = right_height // blk
    rowdev = lax.axis_index("row")
    coldev = lax.axis_index("col")

    own_left, _ = occupied(left_flags(left_pattern, coldev, rowdev, per_k), CAP)
    own_right, _ = occupied(right_flags(right_pattern, coldev, rowdev, trows), CAP)
    left_small = pick_cols(left_rows, own_left, blk)
    right_small = pick_rows(right_cols, own_right, blk)

    roots = [(coldev * ratio + step) % nrow for step in range(STEPS)]
    slots = jnp.stack([jnp.where(rowdev == root, left_small, jnp.zeros_like(left_small)) for root in roots])
    lefts = lax.psum(slots, "row")

    total = jnp.zeros((lrows, blk), jnp.float32)
    highest = lax.Precision.HIGHEST
    for step in range(STEPS):
        shift = step // ratio
        right = right_small if shift == 0 else from_behind(right_small, "col", shift)
        panel = roots[step]
        lidx, lok = occupied(left_flags(left_pattern, coldev, panel, per_k), CAP)
        ridx, rok = occupied(right_flags(right_pattern, (coldev + shift) % ncol, rowdev, trows), CAP)
        match = ((lidx[:, None] == ridx[None, :]) & lok[:, None] & rok[None, :]).astype(jnp.float32)
        left = lefts[step]
        blocks = [left[:, i * blk:(i + 1) * blk] for i in range(CAP)]
        aligned = []
        for j in range(CAP):
            part = match[0, j] * blocks[0]
            for i in range(1, CAP):
                part = part + match[i, j] * blocks[i]
            aligned.append(part)
        aligned = jnp.concatenate(aligned, axis=1)
        total = total + jnp.dot(aligned, right, precision=highest, preferred_element_type=jnp.float32)
    return total


def solution(mesh):
    return jax.shard_map(
        body,
        mesh=mesh,
        in_specs=(P("col", "row"), P("col", "row"), P(), P()),
        out_specs=P("col", "row"),
        check_vma=False,
    )
```

```python
import jax
import jax.numpy as jnp
from jax import lax
from jax.sharding import PartitionSpec as P

STEPS = 4
CAP = 3
QUAD = 4


def shifted(value, axis, steps):
    count = lax.axis_size(axis)
    pairs = [(source, (source - steps) % count) for source in range(count)]
    return lax.ppermute(value, axis, pairs)


def occupied(flags, cap):
    flags = flags != 0
    rank = jnp.cumsum(flags.astype(jnp.int32)) - 1
    where = jnp.arange(flags.shape[0], dtype=jnp.int32)
    hit = flags[None, :] & (rank[None, :] == jnp.arange(cap, dtype=jnp.int32)[:, None])
    index = jnp.sum(jnp.where(hit, where[None, :], 0), axis=1)
    return index, jnp.any(hit, axis=1)


def left_flags(left_pattern, block_row, block_col, per_k):
    return lax.dynamic_slice(left_pattern, (block_row, block_col * per_k), (1, per_k)).reshape(-1)


def right_flags(right_pattern, block_row, block_col, trows):
    return lax.dynamic_slice(right_pattern, (block_row * trows, block_col), (trows, 1)).reshape(-1)


def pick_cols(x, index, blk):
    return jnp.concatenate(
        [lax.dynamic_slice_in_dim(x, index[s] * blk, blk, axis=1) for s in range(index.shape[0])], axis=1
    )


def pick_rows(x, index, blk):
    return jnp.concatenate(
        [lax.dynamic_slice_in_dim(x, index[s] * blk, blk, axis=0) for s in range(index.shape[0])], axis=0
    )


def aligned_left(left, lidx, lok, ridx, rok, blk):
    parts = []
    for j in range(ridx.shape[0]):
        hit = (lidx == ridx[j]) & lok & rok[j]
        source = jnp.sum(jnp.where(hit, jnp.arange(lidx.shape[0], dtype=jnp.int32), 0))
        block = lax.dynamic_slice_in_dim(left, source * blk, blk, axis=1)
        parts.append(jnp.where(jnp.any(hit), block, jnp.zeros_like(block)))
    return jnp.concatenate(parts, axis=1)


def broadcast_lefts(left_small, coldev, rowdev, nrow, ncol):
    spread = nrow // QUAD
    flat = ("row", "col")
    received = []
    for hop in range(1, spread):
        pairs = []
        for c in range(ncol):
            for k in range(STEPS):
                root = (c + k) % nrow
                pairs.append((root * ncol + c, ((root + QUAD * hop) % nrow) * ncol + c))
        received.append(lax.ppermute(left_small, flat, pairs))
    is_root = ((rowdev - coldev) % nrow) < STEPS
    held = received[0]
    for more in received[1:]:
        held = held + more
    held = jnp.where(is_root, left_small, held)
    mine = rowdev % QUAD
    tiles = [held]
    for flip in range(1, QUAD):
        pairs = [(r, (r // QUAD) * QUAD + ((r % QUAD) ^ flip)) for r in range(nrow)]
        tiles.append(lax.ppermute(held, "row", pairs))
    tiles = jnp.stack(tiles)
    lefts = []
    for k in range(STEPS):
        flip = ((coldev + k) % QUAD) ^ mine
        lefts.append(lax.dynamic_index_in_dim(tiles, flip, axis=0, keepdims=False))
    return lefts


def body(left_rows, right_cols, left_pattern, right_pattern):
    nrow = lax.axis_size("row")
    ncol = lax.axis_size("col")
    assert nrow == ncol and nrow % QUAD == 0 and STEPS <= QUAD
    lrows, left_width = left_rows.shape
    right_height, blk = right_cols.shape
    per_k = left_width // blk
    trows = right_height // blk
    rowdev = lax.axis_index("row")
    coldev = lax.axis_index("col")

    own_left, _ = occupied(left_flags(left_pattern, coldev, rowdev, per_k), CAP)
    own_right, rok = occupied(right_flags(right_pattern, coldev, rowdev, trows), CAP)
    left_small = pick_cols(left_rows, own_left, blk)
    right_small = pick_rows(right_cols, own_right, blk)

    lefts = broadcast_lefts(left_small, coldev, rowdev, nrow, ncol)

    highest = lax.Precision.HIGHEST
    total = None
    for step in range(STEPS):
        left = lefts[step] if step == 0 else shifted(lefts[step], "col", -step)
        owner = (coldev - step) % ncol
        lidx, lok = occupied(left_flags(left_pattern, owner, coldev, per_k), CAP)
        aligned = aligned_left(left, lidx, lok, own_right, rok, blk)
        part = jnp.dot(aligned, right_small, precision=highest, preferred_element_type=jnp.float32)
        part = part if step == 0 else shifted(part, "col", step)
        total = part if total is None else total + part
    return total


def solution(mesh):
    return jax.shard_map(
        body,
        mesh=mesh,
        in_specs=(P("col", "row"), P("col", "row"), P(), P()),
        out_specs=P("col", "row"),
        check_vma=False,
    )
```

```python
import jax
import jax.numpy as jnp
from jax import lax
from jax.sharding import PartitionSpec as P

STEPS = 4
CAP = 3
QUAD = 4


def shifted(value, axis, steps):
    count = lax.axis_size(axis)
    pairs = [(source, (source - steps) % count) for source in range(count)]
    return lax.ppermute(value, axis, pairs)


def slots(flags, cap):
    full = (flags != 0).astype(jnp.int32)
    width = full.shape[-1]
    where = jnp.arange(width, dtype=jnp.int32)
    before = (where[None, :] < where[:, None]).astype(jnp.int32)
    rank = jnp.sum(full[:, None, :] * before[None, :, :], axis=-1)
    hit = (full[:, None, :] == 1) & (rank[:, None, :] == jnp.arange(cap, dtype=jnp.int32)[None, :, None])
    index = jnp.sum(jnp.where(hit, where[None, None, :], 0), axis=-1)
    return index, jnp.any(hit, axis=-1)


def pick_cols(x, index, blk):
    return jnp.concatenate(
        [lax.dynamic_slice_in_dim(x, index[s] * blk, blk, axis=1) for s in range(index.shape[0])], axis=1
    )


def pick_rows(x, index, blk):
    return jnp.concatenate(
        [lax.dynamic_slice_in_dim(x, index[s] * blk, blk, axis=0) for s in range(index.shape[0])], axis=0
    )


def aligned_left(left, source, hit, blk):
    parts = []
    for j in range(source.shape[0]):
        block = lax.dynamic_slice_in_dim(left, source[j] * blk, blk, axis=1)
        parts.append(jnp.where(hit[j], block, jnp.zeros_like(block)))
    return jnp.concatenate(parts, axis=1)


def flat_pairs(moves, ncol):
    return [(sr * ncol + sc, dr * ncol + dc) for (sr, sc), (dr, dc) in moves]


def spread_roots(left_small, coldev, rowdev, nrow, ncol):
    flat = ("row", "col")
    received = []
    for hop in range(1, nrow // QUAD):
        moves = []
        for c in range(ncol):
            for k in range(STEPS):
                root = (c + k) % nrow
                moves.append(((root, c), ((root + QUAD * hop) % nrow, c)))
        received.append(lax.ppermute(left_small, flat, flat_pairs(moves, ncol)))
    held = received[0]
    for more in received[1:]:
        held = held + more
    is_root = ((rowdev - coldev) % nrow) < STEPS
    return jnp.where(is_root, left_small, held)


def gather_lefts(held, coldev, rowdev, nrow, ncol):
    flat = ("row", "col")
    flip_here = (coldev % QUAD) ^ (rowdev % QUAD)
    lefts = []
    for k in range(STEPS):
        got = None
        for m in range(QUAD):
            if k == 0 and m == 0:
                continue
            moves = []
            for q in range(ncol):
                for x in range(nrow // QUAD):
                    moves.append(((x * QUAD + q % QUAD, (q - k) % ncol), (x * QUAD + ((q % QUAD) ^ m), q)))
            one = lax.ppermute(held, flat, flat_pairs(moves, ncol))
            got = one if got is None else got + one
        if k == 0:
            got = jnp.where(flip_here == 0, held, got)
        lefts.append(got)
    return lefts


def body(left_rows, right_cols, left_pattern, right_pattern):
    nrow = lax.axis_size("row")
    ncol = lax.axis_size("col")
    assert nrow == ncol and nrow % QUAD == 0 and STEPS <= QUAD
    lrows, left_width = left_rows.shape
    right_height, blk = right_cols.shape
    per_k = left_width // blk
    trows = right_height // blk
    rowdev = lax.axis_index("row")
    coldev = lax.axis_index("col")

    tiles = left_pattern.reshape(ncol, nrow, per_k)
    grid_rows = jnp.stack([coldev] + [(coldev - k) % ncol for k in range(STEPS)])
    panels = jnp.stack([rowdev] + [coldev] * STEPS)
    own_right_flags = lax.dynamic_slice(right_pattern, (coldev * trows, rowdev), (trows, 1)).reshape(1, trows)
    flags = jnp.concatenate([tiles[grid_rows, panels], own_right_flags], axis=0)
    index, ok = slots(flags, CAP)
    own_left = index[0]
    lidx, lok = index[1:1 + STEPS], ok[1:1 + STEPS]
    ridx, rok = index[1 + STEPS], ok[1 + STEPS]
    match = (lidx[:, :, None] == ridx[None, None, :]) & lok[:, :, None] & rok[None, None, :]
    source = jnp.sum(jnp.where(match, jnp.arange(CAP, dtype=jnp.int32)[None, :, None], 0), axis=1)
    hit = jnp.any(match, axis=1)

    left_small = pick_cols(left_rows, own_left, blk)
    right_small = pick_rows(right_cols, ridx, blk)

    held = spread_roots(left_small, coldev, rowdev, nrow, ncol)
    lefts = gather_lefts(held, coldev, rowdev, nrow, ncol)

    highest = lax.Precision.HIGHEST
    total = None
    for step in range(STEPS):
        aligned = aligned_left(lefts[step], source[step], hit[step], blk)
        part = jnp.dot(aligned, right_small, precision=highest, preferred_element_type=jnp.float32)
        part = part if step == 0 else shifted(part, "col", step)
        total = part if total is None else total + part
    return total


def solution(mesh):
    return jax.shard_map(
        body,
        mesh=mesh,
        in_specs=(P("col", "row"), P("col", "row"), P(), P()),
        out_specs=P("col", "row"),
        check_vma=False,
    )
```

```python
import jax
import jax.numpy as jnp
from jax import lax
from jax.sharding import PartitionSpec as P

STEPS = 4
CAP = 3
QUAD = 4


def shifted(value, axis, steps):
    count = lax.axis_size(axis)
    pairs = [(source, (source - steps) % count) for source in range(count)]
    return lax.ppermute(value, axis, pairs)


def slots(flags, cap):
    full = (flags != 0).astype(jnp.int32)
    width = full.shape[-1]
    where = jnp.arange(width, dtype=jnp.int32)
    before = (where[None, :] < where[:, None]).astype(jnp.int32)
    rank = jnp.sum(full[:, None, :] * before[None, :, :], axis=-1)
    hit = (full[:, None, :] == 1) & (rank[:, None, :] == jnp.arange(cap, dtype=jnp.int32)[None, :, None])
    index = jnp.sum(jnp.where(hit, where[None, None, :], 0), axis=-1)
    return index, jnp.any(hit, axis=-1)


def pick_cols(x, index, blk):
    return jnp.concatenate(
        [lax.dynamic_slice_in_dim(x, index[s] * blk, blk, axis=1) for s in range(index.shape[0])], axis=1
    )


def pick_rows(x, index, blk):
    return jnp.concatenate(
        [lax.dynamic_slice_in_dim(x, index[s] * blk, blk, axis=0) for s in range(index.shape[0])], axis=0
    )


def aligned_left(left, source, hit, blk):
    parts = []
    for j in range(source.shape[0]):
        block = lax.dynamic_slice_in_dim(left, source[j] * blk, blk, axis=1)
        parts.append(jnp.where(hit[j], block, jnp.zeros_like(block)))
    return jnp.concatenate(parts, axis=1)


def flat_pairs(moves, ncol):
    return [(sr * ncol + sc, dr * ncol + dc) for (sr, sc), (dr, dc) in moves]


def spread_roots(left_small, coldev, rowdev, nrow, ncol):
    flat = ("row", "col")
    received = []
    for hop in range(1, nrow // QUAD):
        moves = []
        for c in range(ncol):
            for k in range(STEPS):
                root = (c + k) % nrow
                moves.append(((root, c), ((root + QUAD * hop) % nrow, c)))
        received.append(lax.ppermute(left_small, flat, flat_pairs(moves, ncol)))
    held = received[0]
    for more in received[1:]:
        held = held + more
    is_root = ((rowdev - coldev) % nrow) < STEPS
    return jnp.where(is_root, left_small, held)


def gather_lefts(held, coldev, rowdev, nrow, ncol):
    flat = ("row", "col")
    received = []
    for j in range(QUAD):
        moves = []
        for q in range(ncol):
            for x in range(nrow // QUAD):
                for k in range(QUAD):
                    moves.append(((x * QUAD + q % QUAD, (q - k) % ncol), (x * QUAD + (k + j) % QUAD, q)))
        received.append(lax.ppermute(held, flat, flat_pairs(moves, ncol)))
    received = jnp.stack(received)
    slot = rowdev % QUAD
    return [lax.dynamic_index_in_dim(received, (slot - k) % QUAD, axis=0, keepdims=False) for k in range(STEPS)]


def body(left_rows, right_cols, left_pattern, right_pattern):
    nrow = lax.axis_size("row")
    ncol = lax.axis_size("col")
    assert nrow == ncol and nrow % QUAD == 0 and STEPS == QUAD
    lrows, left_width = left_rows.shape
    right_height, blk = right_cols.shape
    per_k = left_width // blk
    trows = right_height // blk
    rowdev = lax.axis_index("row")
    coldev = lax.axis_index("col")

    tiles = left_pattern.reshape(ncol, nrow, per_k)
    grid_rows = jnp.stack([coldev] + [(coldev - k) % ncol for k in range(STEPS)])
    panels = jnp.stack([rowdev] + [coldev] * STEPS)
    own_right_flags = lax.dynamic_slice(right_pattern, (coldev * trows, rowdev), (trows, 1)).reshape(1, trows)
    flags = jnp.concatenate([tiles[grid_rows, panels], own_right_flags], axis=0)
    index, ok = slots(flags, CAP)
    own_left = index[0]
    lidx, lok = index[1:1 + STEPS], ok[1:1 + STEPS]
    ridx, rok = index[1 + STEPS], ok[1 + STEPS]
    match = (lidx[:, :, None] == ridx[None, None, :]) & lok[:, :, None] & rok[None, None, :]
    source = jnp.sum(jnp.where(match, jnp.arange(CAP, dtype=jnp.int32)[None, :, None], 0), axis=1)
    hit = jnp.any(match, axis=1)

    left_small = pick_cols(left_rows, own_left, blk)
    right_small = pick_rows(right_cols, ridx, blk)

    held = spread_roots(left_small, coldev, rowdev, nrow, ncol)
    lefts = gather_lefts(held, coldev, rowdev, nrow, ncol)

    highest = lax.Precision.HIGHEST
    total = None
    for step in range(STEPS):
        aligned = aligned_left(lefts[step], source[step], hit[step], blk)
        part = jnp.dot(aligned, right_small, precision=highest, preferred_element_type=jnp.float32)
        part = part if step == 0 else shifted(part, "col", step)
        total = part if total is None else total + part
    return total


def solution(mesh):
    return jax.shard_map(
        body,
        mesh=mesh,
        in_specs=(P("col", "row"), P("col", "row"), P(), P()),
        out_specs=P("col", "row"),
        check_vma=False,
    )
```

```python
import jax
import jax.numpy as jnp
from jax import lax
from jax.sharding import PartitionSpec as P

STEPS = 4
CAP = 3
QUAD = 4


def shifted(value, axis, steps):
    count = lax.axis_size(axis)
    pairs = [(source, (source - steps) % count) for source in range(count)]
    return lax.ppermute(value, axis, pairs)


def slots(flags, cap):
    full = (flags != 0).astype(jnp.int32)
    width = full.shape[-1]
    where = jnp.arange(width, dtype=jnp.int32)
    before = (where[None, :] < where[:, None]).astype(jnp.int32)
    rank = jnp.sum(full[:, None, :] * before[None, :, :], axis=-1)
    hit = (full[:, None, :] == 1) & (rank[:, None, :] == jnp.arange(cap, dtype=jnp.int32)[None, :, None])
    index = jnp.sum(jnp.where(hit, where[None, None, :], 0), axis=-1)
    return index, jnp.any(hit, axis=-1)


def pick_cols(x, index, blk):
    return jnp.concatenate(
        [lax.dynamic_slice_in_dim(x, index[s] * blk, blk, axis=1) for s in range(index.shape[0])], axis=1
    )


def pick_rows(x, index, blk):
    return jnp.concatenate(
        [lax.dynamic_slice_in_dim(x, index[s] * blk, blk, axis=0) for s in range(index.shape[0])], axis=0
    )


def aligned_left(left, source, hit, blk):
    blocks = [left[:, i * blk:(i + 1) * blk] for i in range(CAP)]
    parts = []
    for j in range(source.shape[0]):
        block = jnp.zeros_like(blocks[0])
        for i in range(CAP):
            block = jnp.where(hit[j] & (source[j] == i), blocks[i], block)
        parts.append(block)
    return jnp.concatenate(parts, axis=1)


def matched(lidx, lok, ridx, rok):
    match = (lidx[:, None] == ridx[None, :]) & lok[:, None] & rok[None, :]
    source = jnp.sum(jnp.where(match, jnp.arange(lidx.shape[0], dtype=jnp.int32)[:, None], 0), axis=0)
    return source, jnp.any(match, axis=0)


def flat_pairs(moves, ncol):
    return [(sr * ncol + sc, dr * ncol + dc) for (sr, sc), (dr, dc) in moves]


def spread_roots(left_small, coldev, rowdev, nrow, ncol):
    flat = ("row", "col")
    received = []
    for hop in range(1, nrow // QUAD):
        moves = []
        for c in range(ncol):
            for k in range(STEPS):
                root = (c + k) % nrow
                moves.append(((root, c), ((root + QUAD * hop) % nrow, c)))
        received.append(lax.ppermute(left_small, flat, flat_pairs(moves, ncol)))
    held = received[0]
    for more in received[1:]:
        held = held + more
    is_root = ((rowdev - coldev) % nrow) < STEPS
    return jnp.where(is_root, left_small, held)


def gather_lefts(held, yhi, nrow, ncol):
    flat = ("row", "col")
    received = []
    for j in range(2):
        moves = []
        for q in range(ncol):
            for x in range(nrow // QUAD):
                for k in range(QUAD):
                    target = x * QUAD + ((k // 2 + j) % 2) * 2 + k % 2
                    moves.append(((x * QUAD + q % QUAD, (q - k) % ncol), (target, q)))
        received.append(lax.ppermute(held, flat, flat_pairs(moves, ncol)))
    near = jnp.where(yhi == 0, received[0], received[1])
    far = jnp.where(yhi == 0, received[1], received[0])
    return near, far


def send_home(part, near_k, to_partner, nrow, ncol):
    flat = ("row", "col")
    moves = []
    for r in range(nrow):
        for q in range(ncol):
            moves.append(((r, q), (r ^ 1 if to_partner else r, (q - r % 2 - near_k) % ncol)))
    return lax.ppermute(part, flat, flat_pairs(moves, ncol))


def body(left_rows, right_cols, left_pattern, right_pattern):
    nrow = lax.axis_size("row")
    ncol = lax.axis_size("col")
    assert nrow == ncol and nrow % QUAD == 0 and STEPS == QUAD == 4
    lrows, left_width = left_rows.shape
    right_height, blk = right_cols.shape
    per_k = left_width // blk
    trows = right_height // blk
    rowdev = lax.axis_index("row")
    coldev = lax.axis_index("col")
    core = rowdev % 2
    yhi = (rowdev // 2) % 2
    partner = rowdev + 1 - 2 * core

    tiles = left_pattern.reshape(ncol, nrow, per_k)
    grid_rows = jnp.stack([coldev] + [(coldev - k) % ncol for k in range(STEPS)])
    panels = jnp.stack([rowdev] + [coldev] * STEPS)
    rights = right_pattern.reshape(ncol, trows, nrow)
    flags = jnp.concatenate(
        [tiles[grid_rows, panels], rights[coldev, :, rowdev][None], rights[coldev, :, partner][None]], axis=0
    )
    index, ok = slots(flags, CAP)
    own_left = index[0]
    lidx, lok = index[1:1 + STEPS], ok[1:1 + STEPS]
    ridx, rok = index[1 + STEPS], ok[1 + STEPS]
    pidx, pok = index[2 + STEPS], ok[2 + STEPS]

    left_small = pick_cols(left_rows, own_left, blk)
    right_small = pick_rows(right_cols, ridx, blk)
    right_partner = lax.ppermute(right_small, "row", [(r, r ^ 1) for r in range(nrow)])

    held = spread_roots(left_small, coldev, rowdev, nrow, ncol)
    near, far = gather_lefts(held, yhi, nrow, ncol)

    highest = lax.Precision.HIGHEST
    total = None
    for near_k, left in ((0, near), (2, far)):
        k = core + near_k
        kl = lax.dynamic_index_in_dim(lidx, k, axis=0, keepdims=False)
        kok = lax.dynamic_index_in_dim(lok, k, axis=0, keepdims=False)
        for to_partner, (bidx, bok, right) in ((False, (ridx, rok, right_small)), (True, (pidx, pok, right_partner))):
            source, hit = matched(kl, kok, bidx, bok)
            aligned = aligned_left(left, source, hit, blk)
            part = jnp.dot(aligned, right, precision=highest, preferred_element_type=jnp.float32)
            part = send_home(part, near_k, to_partner, nrow, ncol)
            total = part if total is None else total + part
    return total


def solution(mesh):
    return jax.shard_map(
        body,
        mesh=mesh,
        in_specs=(P("col", "row"), P("col", "row"), P(), P()),
        out_specs=P("col", "row"),
        check_vma=False,
    )
```

```python
import jax
import jax.numpy as jnp
from jax import lax
from jax.sharding import PartitionSpec as P

STEPS = 4
CAP = 3
QUAD = 4


def shifted(value, axis, steps):
    count = lax.axis_size(axis)
    pairs = [(source, (source - steps) % count) for source in range(count)]
    return lax.ppermute(value, axis, pairs)


def slots(flags, cap):
    full = (flags != 0).astype(jnp.int32)
    width = full.shape[-1]
    where = jnp.arange(width, dtype=jnp.int32)
    before = (where[None, :] < where[:, None]).astype(jnp.int32)
    rank = jnp.sum(full[:, None, :] * before[None, :, :], axis=-1)
    hit = (full[:, None, :] == 1) & (rank[:, None, :] == jnp.arange(cap, dtype=jnp.int32)[None, :, None])
    index = jnp.sum(jnp.where(hit, where[None, None, :], 0), axis=-1)
    return index, jnp.any(hit, axis=-1)


def pick_cols(x, index, blk):
    return jnp.concatenate(
        [lax.dynamic_slice_in_dim(x, index[s] * blk, blk, axis=1) for s in range(index.shape[0])], axis=1
    )


def pick_rows(x, index, blk):
    return jnp.concatenate(
        [lax.dynamic_slice_in_dim(x, index[s] * blk, blk, axis=0) for s in range(index.shape[0])], axis=0
    )


def aligned_left(left, source, hit, blk):
    weight = (hit[:, None] & (source[:, None] == jnp.arange(CAP, dtype=jnp.int32)[None, :])).astype(left.dtype)
    blocks = [left[:, i * blk:(i + 1) * blk] for i in range(CAP)]
    parts = []
    for j in range(source.shape[0]):
        block = weight[j, 0] * blocks[0]
        for i in range(1, CAP):
            block = block + weight[j, i] * blocks[i]
        parts.append(block)
    return jnp.concatenate(parts, axis=1)


def matched(lidx, lok, ridx, rok):
    match = (lidx[:, None] == ridx[None, :]) & lok[:, None] & rok[None, :]
    source = jnp.sum(jnp.where(match, jnp.arange(lidx.shape[0], dtype=jnp.int32)[:, None], 0), axis=0)
    return source, jnp.any(match, axis=0)


def flat_pairs(moves, ncol):
    return [(sr * ncol + sc, dr * ncol + dc) for (sr, sc), (dr, dc) in moves]


def spread_roots(left_small, coldev, rowdev, nrow, ncol):
    flat = ("row", "col")
    received = []
    for hop in range(1, nrow // QUAD):
        moves = []
        for c in range(ncol):
            for k in range(STEPS):
                root = (c + k) % nrow
                moves.append(((root, c), ((root + QUAD * hop) % nrow, c)))
        received.append(lax.ppermute(left_small, flat, flat_pairs(moves, ncol)))
    held = received[0]
    for more in received[1:]:
        held = held + more
    is_root = ((rowdev - coldev) % nrow) < STEPS
    return jnp.where(is_root, left_small, held)


def gather_lefts(held, yhi, nrow, ncol):
    flat = ("row", "col")
    received = []
    for j in range(2):
        moves = []
        for q in range(ncol):
            for x in range(nrow // QUAD):
                for k in range(QUAD):
                    target = x * QUAD + ((k // 2 + j) % 2) * 2 + k % 2
                    moves.append(((x * QUAD + q % QUAD, (q - k) % ncol), (target, q)))
        received.append(lax.ppermute(held, flat, flat_pairs(moves, ncol)))
    near = jnp.where(yhi == 0, received[0], received[1])
    far = jnp.where(yhi == 0, received[1], received[0])
    return near, far


def send_home(part, near_k, to_partner, nrow, ncol):
    flat = ("row", "col")
    moves = []
    for r in range(nrow):
        for q in range(ncol):
            moves.append(((r, q), (r ^ 1 if to_partner else r, (q - r % 2 - near_k) % ncol)))
    return lax.ppermute(part, flat, flat_pairs(moves, ncol))


def body(left_rows, right_cols, left_pattern, right_pattern):
    nrow = lax.axis_size("row")
    ncol = lax.axis_size("col")
    assert nrow == ncol and nrow % QUAD == 0 and STEPS == QUAD == 4
    lrows, left_width = left_rows.shape
    right_height, blk = right_cols.shape
    per_k = left_width // blk
    trows = right_height // blk
    rowdev = lax.axis_index("row")
    coldev = lax.axis_index("col")
    core = rowdev % 2
    yhi = (rowdev // 2) % 2
    partner = rowdev + 1 - 2 * core

    tiles = left_pattern.reshape(ncol, nrow, per_k)
    grid_rows = jnp.stack([coldev] + [(coldev - k) % ncol for k in range(STEPS)])
    panels = jnp.stack([rowdev] + [coldev] * STEPS)
    rights = right_pattern.reshape(ncol, trows, nrow)
    flags = jnp.concatenate(
        [tiles[grid_rows, panels], rights[coldev, :, rowdev][None], rights[coldev, :, partner][None]], axis=0
    )
    index, ok = slots(flags, CAP)
    own_left = index[0]
    lidx, lok = index[1:1 + STEPS], ok[1:1 + STEPS]
    ridx, rok = index[1 + STEPS], ok[1 + STEPS]
    pidx, pok = index[2 + STEPS], ok[2 + STEPS]

    left_small = pick_cols(left_rows, own_left, blk)
    right_small = pick_rows(right_cols, ridx, blk)
    right_partner = lax.ppermute(right_small, "row", [(r, r ^ 1) for r in range(nrow)])

    held = spread_roots(left_small, coldev, rowdev, nrow, ncol)
    near, far = gather_lefts(held, yhi, nrow, ncol)

    highest = lax.Precision.HIGHEST
    total = None
    for near_k, left in ((0, near), (2, far)):
        k = core + near_k
        kl = lax.dynamic_index_in_dim(lidx, k, axis=0, keepdims=False)
        kok = lax.dynamic_index_in_dim(lok, k, axis=0, keepdims=False)
        for to_partner, (bidx, bok, right) in ((False, (ridx, rok, right_small)), (True, (pidx, pok, right_partner))):
            source, hit = matched(kl, kok, bidx, bok)
            aligned = aligned_left(left, source, hit, blk)
            part = jnp.dot(aligned, right, precision=highest, preferred_element_type=jnp.float32)
            part = send_home(part, near_k, to_partner, nrow, ncol)
            total = part if total is None else total + part
    return total


def solution(mesh):
    return jax.shard_map(
        body,
        mesh=mesh,
        in_specs=(P("col", "row"), P("col", "row"), P(), P()),
        out_specs=P("col", "row"),
        check_vma=False,
    )
```

```python
import jax
import jax.numpy as jnp
from jax import lax
from jax.sharding import PartitionSpec as P

STEPS = 4
CAP = 3
QUAD = 4


def shifted(value, axis, steps):
    count = lax.axis_size(axis)
    pairs = [(source, (source - steps) % count) for source in range(count)]
    return lax.ppermute(value, axis, pairs)


def slots(flags, cap):
    full = (flags != 0).astype(jnp.int32)
    width = full.shape[-1]
    where = jnp.arange(width, dtype=jnp.int32)
    before = (where[None, :] < where[:, None]).astype(jnp.int32)
    rank = jnp.sum(full[:, None, :] * before[None, :, :], axis=-1)
    hit = (full[:, None, :] == 1) & (rank[:, None, :] == jnp.arange(cap, dtype=jnp.int32)[None, :, None])
    index = jnp.sum(jnp.where(hit, where[None, None, :], 0), axis=-1)
    return index, jnp.any(hit, axis=-1)


def pick_cols(x, index, blk):
    return jnp.concatenate(
        [lax.dynamic_slice_in_dim(x, index[s] * blk, blk, axis=1) for s in range(index.shape[0])], axis=1
    )


def pick_rows(x, index, blk):
    return jnp.concatenate(
        [lax.dynamic_slice_in_dim(x, index[s] * blk, blk, axis=0) for s in range(index.shape[0])], axis=0
    )


def aligned_right(right, lidx, lok, ridx, rok, blk):
    weight = ((lidx[:, None] == ridx[None, :]) & lok[:, None] & rok[None, :]).astype(right.dtype)
    blocks = right.reshape(ridx.shape[0], blk, right.shape[1])
    picked = jnp.einsum("ij,jab->iab", weight, blocks, precision=lax.Precision.HIGHEST)
    return picked.reshape(right.shape)


def flat_pairs(moves, ncol):
    return [(sr * ncol + sc, dr * ncol + dc) for (sr, sc), (dr, dc) in moves]


def spread_roots(left_small, coldev, rowdev, nrow, ncol):
    flat = ("row", "col")
    received = []
    for hop in range(1, nrow // QUAD):
        moves = []
        for c in range(ncol):
            for k in range(STEPS):
                root = (c + k) % nrow
                moves.append(((root, c), ((root + QUAD * hop) % nrow, c)))
        received.append(lax.ppermute(left_small, flat, flat_pairs(moves, ncol)))
    held = received[0]
    for more in received[1:]:
        held = held + more
    is_root = ((rowdev - coldev) % nrow) < STEPS
    return jnp.where(is_root, left_small, held)


def gather_lefts(held, yhi, nrow, ncol):
    flat = ("row", "col")
    received = []
    for j in range(2):
        moves = []
        for q in range(ncol):
            for x in range(nrow // QUAD):
                for k in range(QUAD):
                    target = x * QUAD + ((k // 2 + j) % 2) * 2 + k % 2
                    moves.append(((x * QUAD + q % QUAD, (q - k) % ncol), (target, q)))
        received.append(lax.ppermute(held, flat, flat_pairs(moves, ncol)))
    near = jnp.where(yhi == 0, received[0], received[1])
    far = jnp.where(yhi == 0, received[1], received[0])
    return near, far


def send_home(part, near_k, to_partner, nrow, ncol):
    flat = ("row", "col")
    moves = []
    for r in range(nrow):
        for q in range(ncol):
            moves.append(((r, q), (r ^ 1 if to_partner else r, (q - r % 2 - near_k) % ncol)))
    return lax.ppermute(part, flat, flat_pairs(moves, ncol))


def body(left_rows, right_cols, left_pattern, right_pattern):
    nrow = lax.axis_size("row")
    ncol = lax.axis_size("col")
    assert nrow == ncol and nrow % QUAD == 0 and STEPS == QUAD == 4
    lrows, left_width = left_rows.shape
    right_height, blk = right_cols.shape
    per_k = left_width // blk
    trows = right_height // blk
    rowdev = lax.axis_index("row")
    coldev = lax.axis_index("col")
    core = rowdev % 2
    yhi = (rowdev // 2) % 2

    tiles = left_pattern.reshape(ncol, nrow, per_k)
    grid_rows = jnp.stack([coldev] + [(coldev - k) % ncol for k in range(STEPS)])
    panels = jnp.stack([rowdev] + [coldev] * STEPS)
    rights = right_pattern.reshape(ncol, trows, nrow)
    flags = jnp.concatenate([tiles[grid_rows, panels], rights[coldev, :, rowdev][None]], axis=0)
    index, ok = slots(flags, CAP)
    own_left = index[0]
    lidx, lok = index[1:1 + STEPS], ok[1:1 + STEPS]
    ridx, rok = index[1 + STEPS], ok[1 + STEPS]

    left_small = pick_cols(left_rows, own_left, blk)
    right_small = pick_rows(right_cols, ridx, blk)
    highest = lax.Precision.HIGHEST

    def ordered_for(k):
        kl = lax.dynamic_index_in_dim(lidx, k, axis=0, keepdims=False)
        kok = lax.dynamic_index_in_dim(lok, k, axis=0, keepdims=False)
        return aligned_right(right_small, kl, kok, ridx, rok, blk)

    for_partner = jnp.stack([ordered_for(1 - core), ordered_for(3 - core)])
    from_partner = lax.ppermute(for_partner, "row", [(r, r ^ 1) for r in range(nrow)])
    plans = [
        (0, False, ordered_for(core)),
        (2, False, ordered_for(core + 2)),
        (0, True, from_partner[0]),
        (2, True, from_partner[1]),
    ]

    held = spread_roots(left_small, coldev, rowdev, nrow, ncol)
    near, far = gather_lefts(held, yhi, nrow, ncol)

    total = None
    for near_k, to_partner, right in plans:
        left = near if near_k == 0 else far
        part = jnp.dot(left, right, precision=highest, preferred_element_type=jnp.float32)
        part = send_home(part, near_k, to_partner, nrow, ncol)
        total = part if total is None else total + part
    return total


def solution(mesh):
    return jax.shard_map(
        body,
        mesh=mesh,
        in_specs=(P("col", "row"), P("col", "row"), P(), P()),
        out_specs=P("col", "row"),
        check_vma=False,
    )
```

```python
import jax
import jax.numpy as jnp
from jax import lax
from jax.sharding import PartitionSpec as P


STEPS = 4
CAP = 3
QUAD = 4


def slots(flags, cap):
    full = (flags != 0).astype(jnp.int32)
    width = full.shape[-1]
    where = jnp.arange(width, dtype=jnp.int32)
    before = (where[None, :] < where[:, None]).astype(jnp.int32)
    rank = jnp.sum(full[:, None, :] * before[None, :, :], axis=-1)
    hit = (full[:, None, :] == 1) & (rank[:, None, :] == jnp.arange(cap, dtype=jnp.int32)[None, :, None])
    index = jnp.sum(jnp.where(hit, where[None, None, :], 0), axis=-1)
    return index, jnp.any(hit, axis=-1)


def pick_cols(x, index, blk):
    return jnp.concatenate(
        [lax.dynamic_slice_in_dim(x, index[s] * blk, blk, axis=1) for s in range(index.shape[0])], axis=1
    )


def pick_rows(x, index, blk):
    return jnp.concatenate(
        [lax.dynamic_slice_in_dim(x, index[s] * blk, blk, axis=0) for s in range(index.shape[0])], axis=0
    )


def aligned_right(right, lidx, lok, ridx, rok, blk):
    weight = ((lidx[:, None] == ridx[None, :]) & lok[:, None] & rok[None, :]).astype(right.dtype)
    blocks = right.reshape(ridx.shape[0], blk, right.shape[1])
    picked = jnp.einsum("ij,jab->iab", weight, blocks, precision=lax.Precision.HIGHEST)
    return picked.reshape(right.shape)


def flat_pairs(moves, ncol):
    return [(sr * ncol + sc, dr * ncol + dc) for (sr, sc), (dr, dc) in moves]


def spread_roots(left_small, coldev, rowdev, nrow, ncol):
    flat = ("row", "col")
    received = []
    for hop in range(1, nrow // QUAD):
        moves = []
        for c in range(ncol):
            for k in range(STEPS):
                root = (c + k) % nrow
                moves.append(((root, c), ((root + QUAD * hop) % nrow, c)))
        received.append(lax.ppermute(left_small, flat, flat_pairs(moves, ncol)))
    held = received[0]
    for more in received[1:]:
        held = held + more
    is_root = ((rowdev - coldev) % nrow) < STEPS
    return jnp.where(is_root, left_small, held)


def gather_lefts(held, yhi, nrow, ncol):
    flat = ("row", "col")
    received = []
    for j in range(2):
        moves = []
        for q in range(ncol):
            for x in range(nrow // QUAD):
                for k in range(QUAD):
                    target = x * QUAD + ((k // 2 + j) % 2) * 2 + k % 2
                    moves.append(((x * QUAD + q % QUAD, (q - k) % ncol), (target, q)))
        received.append(lax.ppermute(held, flat, flat_pairs(moves, ncol)))
    near = jnp.where(yhi == 0, received[0], received[1])
    far = jnp.where(yhi == 0, received[1], received[0])
    return near, far


def send_home(part, near_k, to_partner, nrow, ncol):
    flat = ("row", "col")
    moves = []
    for r in range(nrow):
        for q in range(ncol):
            moves.append(((r, q), (r ^ 1 if to_partner else r, (q - r % 2 - near_k) % ncol)))
    return lax.ppermute(part, flat, flat_pairs(moves, ncol))


def steps(left_rows, right_cols, left_pattern, right_pattern):
    nrow = lax.axis_size("row")
    ncol = lax.axis_size("col")
    assert nrow == ncol and nrow % QUAD == 0 and STEPS == QUAD == 4
    _, left_width = left_rows.shape
    right_height, blk = right_cols.shape
    per_k = left_width // blk
    trows = right_height // blk
    rowdev = lax.axis_index("row")
    coldev = lax.axis_index("col")
    core = rowdev % 2
    yhi = (rowdev // 2) % 2

    tiles = left_pattern.reshape(ncol, nrow, per_k)
    grid_rows = jnp.stack([coldev] + [(coldev - k) % ncol for k in range(STEPS)])
    panels = jnp.stack([rowdev] + [coldev] * STEPS)
    rights = right_pattern.reshape(ncol, trows, nrow)
    flags = jnp.concatenate([tiles[grid_rows, panels], rights[coldev, :, rowdev][None]], axis=0)
    index, ok = slots(flags, CAP)
    own_left = index[0]
    lidx, lok = index[1:1 + STEPS], ok[1:1 + STEPS]
    ridx, rok = index[1 + STEPS], ok[1 + STEPS]

    left_small = pick_cols(left_rows, own_left, blk)
    right_small = pick_rows(right_cols, ridx, blk)
    highest = lax.Precision.HIGHEST

    def ordered_for(k):
        kl = lax.dynamic_index_in_dim(lidx, k, axis=0, keepdims=False)
        kok = lax.dynamic_index_in_dim(lok, k, axis=0, keepdims=False)
        return aligned_right(right_small, kl, kok, ridx, rok, blk)

    for_partner = jnp.stack([ordered_for(1 - core), ordered_for(3 - core)])
    from_partner = lax.ppermute(for_partner, "row", [(r, r ^ 1) for r in range(nrow)])
    plans = [
        (0, False, ordered_for(core)),
        (2, False, ordered_for(core + 2)),
        (0, True, from_partner[0]),
        (2, True, from_partner[1]),
    ]

    held = spread_roots(left_small, coldev, rowdev, nrow, ncol)
    near, far = gather_lefts(held, yhi, nrow, ncol)

    total = None
    for near_k, to_partner, right in plans:
        left = near if near_k == 0 else far
        part = jnp.dot(left, right, precision=highest, preferred_element_type=jnp.float32)
        part = send_home(part, near_k, to_partner, nrow, ncol)
        total = part if total is None else total + part
    return total


def solution(mesh):
    return jax.shard_map(
        steps,
        mesh=mesh,
        in_specs=(P("col", "row"), P("col", "row"), P(), P()),
        out_specs=P("col", "row"),
        check_vma=False,
    )
```

```python
import jax
import jax.numpy as jnp
from jax import lax
from jax.sharding import PartitionSpec as P


STEPS = 4
CAP = 3
QUAD = 4


def slots(flags, cap):
    full = (flags != 0).astype(jnp.int32)
    width = full.shape[-1]
    where = jnp.arange(width, dtype=jnp.int32)
    before = (where[None, :] < where[:, None]).astype(jnp.int32)
    rank = jnp.sum(full[:, None, :] * before[None, :, :], axis=-1)
    hit = (full[:, None, :] == 1) & (rank[:, None, :] == jnp.arange(cap, dtype=jnp.int32)[None, :, None])
    index = jnp.sum(jnp.where(hit, where[None, None, :], 0), axis=-1)
    return index, jnp.any(hit, axis=-1)


def pick_cols(x, index, blk):
    return jnp.concatenate(
        [lax.dynamic_slice_in_dim(x, index[s] * blk, blk, axis=1) for s in range(index.shape[0])], axis=1
    )


def pick_rows(x, index, blk):
    return jnp.concatenate(
        [lax.dynamic_slice_in_dim(x, index[s] * blk, blk, axis=0) for s in range(index.shape[0])], axis=0
    )


def aligned_right(right, lidx, lok, ridx, rok, blk):
    weight = ((lidx[:, None] == ridx[None, :]) & lok[:, None] & rok[None, :]).astype(right.dtype)
    blocks = right.reshape(ridx.shape[0], blk, right.shape[1])
    picked = jnp.einsum("ij,jab->iab", weight, blocks, precision=lax.Precision.HIGHEST)
    return picked.reshape(right.shape)


def flat_pairs(moves, ncol):
    return [(sr * ncol + sc, dr * ncol + dc) for (sr, sc), (dr, dc) in moves]


def spread_roots(left_small, coldev, rowdev, nrow, ncol):
    flat = ("row", "col")
    received = []
    for hop in range(1, nrow // QUAD):
        moves = []
        for c in range(ncol):
            for k in range(STEPS):
                root = (c + k) % nrow
                moves.append(((root, c), ((root + QUAD * hop) % nrow, c)))
        received.append(lax.ppermute(left_small, flat, flat_pairs(moves, ncol)))
    held = received[0]
    for more in received[1:]:
        held = held + more
    is_root = ((rowdev - coldev) % nrow) < STEPS
    return jnp.where(is_root, left_small, held)


def gather_lefts(held, yhi, nrow, ncol):
    flat = ("row", "col")
    received = []
    for j in range(2):
        moves = []
        for q in range(ncol):
            for x in range(nrow // QUAD):
                for k in range(QUAD):
                    target = x * QUAD + ((k // 2 + j) % 2) * 2 + k % 2
                    moves.append(((x * QUAD + q % QUAD, (q - k) % ncol), (target, q)))
        received.append(lax.ppermute(held, flat, flat_pairs(moves, ncol)))
    near = jnp.where(yhi == 0, received[0], received[1])
    far = jnp.where(yhi == 0, received[1], received[0])
    return near, far


def send_home(part, near_k, to_partner, nrow, ncol):
    flat = ("row", "col")
    moves = []
    for r in range(nrow):
        for q in range(ncol):
            moves.append(((r, q), (r ^ 1 if to_partner else r, (q - r % 2 - near_k) % ncol)))
    return lax.ppermute(part, flat, flat_pairs(moves, ncol))


def steps(left_rows, right_cols, left_pattern, right_pattern):
    nrow = lax.axis_size("row")
    ncol = lax.axis_size("col")
    assert nrow == ncol and nrow % QUAD == 0 and STEPS == QUAD == 4
    _, left_width = left_rows.shape
    right_height, blk = right_cols.shape
    per_k = left_width // blk
    trows = right_height // blk
    rowdev = lax.axis_index("row")
    coldev = lax.axis_index("col")
    core = rowdev % 2
    yhi = (rowdev // 2) % 2

    grid_rows = jnp.stack([coldev] + [(coldev - k) % ncol for k in range(STEPS)])
    panels = jnp.stack([rowdev] + [coldev] * STEPS)
    lefts = left_pattern[grid_rows[:, None], panels[:, None] * per_k + jnp.arange(per_k)[None, :]]
    own_right = lax.dynamic_slice(right_pattern, (coldev * trows, rowdev), (trows, 1)).reshape(1, trows)
    flags = jnp.concatenate([lefts, own_right], axis=0)
    index, ok = slots(flags, CAP)
    own_left = index[0]
    lidx, lok = index[1:1 + STEPS], ok[1:1 + STEPS]
    ridx, rok = index[1 + STEPS], ok[1 + STEPS]

    left_small = pick_cols(left_rows, own_left, blk)
    right_small = pick_rows(right_cols, ridx, blk)
    highest = lax.Precision.HIGHEST

    def ordered_for(k):
        kl = lax.dynamic_index_in_dim(lidx, k, axis=0, keepdims=False)
        kok = lax.dynamic_index_in_dim(lok, k, axis=0, keepdims=False)
        return aligned_right(right_small, kl, kok, ridx, rok, blk)

    for_partner = jnp.stack([ordered_for(1 - core), ordered_for(3 - core)])
    from_partner = lax.ppermute(for_partner, "row", [(r, r ^ 1) for r in range(nrow)])
    own_near, own_far = ordered_for(core), ordered_for(core + 2)
    plans = [(0, False, own_near), (2, False, own_far), (0, True, from_partner[0]), (2, True, from_partner[1])]

    held = spread_roots(left_small, coldev, rowdev, nrow, ncol)
    near, far = gather_lefts(held, yhi, nrow, ncol)

    total = None
    for near_k, to_partner, right in plans:
        left = near if near_k == 0 else far
        part = jnp.dot(left, right, precision=highest, preferred_element_type=jnp.float32)
        part = send_home(part, near_k, to_partner, nrow, ncol)
        total = part if total is None else total + part
    return total


def solution(mesh):
    return jax.shard_map(
        steps,
        mesh=mesh,
        in_specs=(P("col", "row"), P("col", "row"), P(), P()),
        out_specs=P("col", "row"),
        check_vma=False,
    )
```

```python
import jax
import jax.numpy as jnp
from jax import lax
from jax.sharding import PartitionSpec as P


STEPS = 4
CAP = 3
QUAD = 4


def slots(flags, cap):
    full = (flags != 0).astype(jnp.int32)
    width = full.shape[-1]
    where = jnp.arange(width, dtype=jnp.int32)
    before = (where[None, :] < where[:, None]).astype(jnp.int32)
    rank = jnp.sum(full[:, None, :] * before[None, :, :], axis=-1)
    hit = (full[:, None, :] == 1) & (rank[:, None, :] == jnp.arange(cap, dtype=jnp.int32)[None, :, None])
    index = jnp.sum(jnp.where(hit, where[None, None, :], 0), axis=-1)
    return index, jnp.any(hit, axis=-1)


def pick_cols(x, index, blk):
    return jnp.concatenate(
        [lax.dynamic_slice_in_dim(x, index[s] * blk, blk, axis=1) for s in range(index.shape[0])], axis=1
    )


def pick_rows(x, index, blk):
    return jnp.concatenate(
        [lax.dynamic_slice_in_dim(x, index[s] * blk, blk, axis=0) for s in range(index.shape[0])], axis=0
    )


def aligned_right(right, lidx, lok, ridx, rok, blk):
    weight = ((lidx[:, None] == ridx[None, :]) & lok[:, None] & rok[None, :]).astype(right.dtype)
    blocks = right.reshape(ridx.shape[0], blk, right.shape[1])
    picked = jnp.einsum("ij,jab->iab", weight, blocks, precision=lax.Precision.HIGHEST)
    return picked.reshape(right.shape)


def flat_pairs(moves, ncol):
    return [(sr * ncol + sc, dr * ncol + dc) for (sr, sc), (dr, dc) in moves]


def spread_roots(left_small, coldev, rowdev, nrow, ncol):
    flat = ("row", "col")
    received = []
    for hop in range(1, nrow // QUAD):
        moves = []
        for c in range(ncol):
            for k in range(STEPS):
                root = (c + k) % nrow
                moves.append(((root, c), ((root + QUAD * hop) % nrow, c)))
        received.append(lax.ppermute(left_small, flat, flat_pairs(moves, ncol)))
    held = received[0]
    for more in received[1:]:
        held = held + more
    is_root = ((rowdev - coldev) % nrow) < STEPS
    return jnp.where(is_root, left_small, held)


def gather_lefts(held, nrow, ncol):
    flat = ("row", "col")
    received = []
    for j in range(2):
        moves = []
        for q in range(ncol):
            for x in range(nrow // QUAD):
                for k in range(QUAD):
                    target = x * QUAD + ((k // 2 + j) % 2) * 2 + k % 2
                    moves.append(((x * QUAD + q % QUAD, (q - k) % ncol), (target, q)))
        received.append(lax.ppermute(held, flat, flat_pairs(moves, ncol)))
    return received


def tile_of(row, j):
    return row % 2 + 2 * (((row // 2) % 2 + j) % 2)


def send_home(part, j, to_partner, nrow, ncol):
    flat = ("row", "col")
    moves = []
    for r in range(nrow):
        for q in range(ncol):
            moves.append(((r, q), (r ^ 1 if to_partner else r, (q - tile_of(r, j)) % ncol)))
    return lax.ppermute(part, flat, flat_pairs(moves, ncol))


def steps(left_rows, right_cols, left_pattern, right_pattern):
    nrow = lax.axis_size("row")
    ncol = lax.axis_size("col")
    assert nrow == ncol and nrow % QUAD == 0 and STEPS == QUAD == 4
    _, left_width = left_rows.shape
    right_height, blk = right_cols.shape
    per_k = left_width // blk
    trows = right_height // blk
    rowdev = lax.axis_index("row")
    coldev = lax.axis_index("col")

    own_flags = lax.dynamic_slice(left_pattern, (coldev, rowdev * per_k), (1, per_k))
    own_left = slots(own_flags, CAP)[0][0]
    grid_rows = jnp.stack([(coldev - k) % ncol for k in range(STEPS)])
    lefts = left_pattern[grid_rows[:, None], coldev * per_k + jnp.arange(per_k)[None, :]]
    own_right = lax.dynamic_slice(right_pattern, (coldev * trows, rowdev), (trows, 1)).reshape(1, trows)
    index, ok = slots(jnp.concatenate([lefts, own_right], axis=0), CAP)
    lidx, lok = index[:STEPS], ok[:STEPS]
    ridx, rok = index[STEPS], ok[STEPS]

    left_small = pick_cols(left_rows, own_left, blk)
    right_small = pick_rows(right_cols, ridx, blk)
    highest = lax.Precision.HIGHEST

    def ordered_for(k):
        kl = lax.dynamic_index_in_dim(lidx, k, axis=0, keepdims=False)
        kok = lax.dynamic_index_in_dim(lok, k, axis=0, keepdims=False)
        return aligned_right(right_small, kl, kok, ridx, rok, blk)

    for_partner = jnp.stack([ordered_for(tile_of(rowdev ^ 1, j)) for j in range(2)])
    from_partner = lax.ppermute(for_partner, "row", [(r, r ^ 1) for r in range(nrow)])
    own = [ordered_for(tile_of(rowdev, j)) for j in range(2)]

    held = spread_roots(left_small, coldev, rowdev, nrow, ncol)
    received = gather_lefts(held, nrow, ncol)

    total = None
    for j in range(2):
        for to_partner, right in ((False, own[j]), (True, from_partner[j])):
            part = jnp.dot(received[j], right, precision=highest, preferred_element_type=jnp.float32)
            part = send_home(part, j, to_partner, nrow, ncol)
            total = part if total is None else total + part
    return total


def solution(mesh):
    return jax.shard_map(
        steps,
        mesh=mesh,
        in_specs=(P("col", "row"), P("col", "row"), P(), P()),
        out_specs=P("col", "row"),
        check_vma=False,
    )
```

```python
import jax
import jax.numpy as jnp
from jax import lax
from jax.sharding import PartitionSpec as P


STEPS = 4
CAP = 3
QUAD = 4


def shifted(value, axis, steps):
    count = lax.axis_size(axis)
    pairs = [(source, (source - steps) % count) for source in range(count)]
    return lax.ppermute(value, axis, pairs)


def slots(flags, cap):
    full = (flags != 0).astype(jnp.int32)
    width = full.shape[-1]
    where = jnp.arange(width, dtype=jnp.int32)
    before = (where[None, :] < where[:, None]).astype(jnp.int32)
    rank = jnp.sum(full[:, None, :] * before[None, :, :], axis=-1)
    hit = (full[:, None, :] == 1) & (rank[:, None, :] == jnp.arange(cap, dtype=jnp.int32)[None, :, None])
    index = jnp.sum(jnp.where(hit, where[None, None, :], 0), axis=-1)
    return index, jnp.any(hit, axis=-1)


def pick_cols(x, index, blk):
    return jnp.concatenate(
        [lax.dynamic_slice_in_dim(x, index[s] * blk, blk, axis=1) for s in range(index.shape[0])], axis=1
    )


def pick_rows(x, index, blk):
    return jnp.concatenate(
        [lax.dynamic_slice_in_dim(x, index[s] * blk, blk, axis=0) for s in range(index.shape[0])], axis=0
    )


def aligned_right(right, lidx, lok, ridx, rok, blk):
    weight = ((lidx[:, None] == ridx[None, :]) & lok[:, None] & rok[None, :]).astype(right.dtype)
    blocks = right.reshape(ridx.shape[0], blk, right.shape[1])
    picked = jnp.einsum("ij,jab->iab", weight, blocks, precision=lax.Precision.HIGHEST)
    return picked.reshape(right.shape)


def flat_pairs(moves, ncol):
    return [(sr * ncol + sc, dr * ncol + dc) for (sr, sc), (dr, dc) in moves]


def spread_roots(left_small, coldev, rowdev, nrow, ncol):
    flat = ("row", "col")
    received = []
    for hop in range(1, nrow // QUAD):
        moves = []
        for c in range(ncol):
            for k in range(STEPS):
                root = (c + k) % nrow
                moves.append(((root, c), ((root + QUAD * hop) % nrow, c)))
        received.append(lax.ppermute(left_small, flat, flat_pairs(moves, ncol)))
    held = received[0]
    for more in received[1:]:
        held = held + more
    is_root = ((rowdev - coldev) % nrow) < STEPS
    return jnp.where(is_root, left_small, held)


def gather_lefts(held, yhi, nrow, ncol):
    flat = ("row", "col")
    received = []
    for j in range(2):
        moves = []
        for q in range(ncol):
            for x in range(nrow // QUAD):
                for k in range(QUAD):
                    target = x * QUAD + ((k // 2 + j) % 2) * 2 + k % 2
                    moves.append(((x * QUAD + q % QUAD, (q - k) % ncol), (target, q)))
        received.append(lax.ppermute(held, flat, flat_pairs(moves, ncol)))
    near = jnp.where(yhi == 0, received[0], received[1])
    far = jnp.where(yhi == 0, received[1], received[0])
    return near, far


def steps(left_rows, right_cols, left_pattern, right_pattern):
    nrow = lax.axis_size("row")
    ncol = lax.axis_size("col")
    assert nrow == ncol and nrow % QUAD == 0 and STEPS == QUAD == 4
    _, left_width = left_rows.shape
    right_height, blk = right_cols.shape
    per_k = left_width // blk
    trows = right_height // blk
    rowdev = lax.axis_index("row")
    coldev = lax.axis_index("col")
    core = rowdev % 2
    yhi = (rowdev // 2) % 2

    own_flags = lax.dynamic_slice(left_pattern, (coldev, rowdev * per_k), (1, per_k))
    own_left = slots(own_flags, CAP)[0][0]
    grid_rows = jnp.stack([(coldev - k) % ncol for k in range(STEPS)])
    lefts = left_pattern[grid_rows[:, None], coldev * per_k + jnp.arange(per_k)[None, :]]
    own_right = lax.dynamic_slice(right_pattern, (coldev * trows, rowdev), (trows, 1)).reshape(1, trows)
    index, ok = slots(jnp.concatenate([lefts, own_right], axis=0), CAP)
    lidx, lok = index[:STEPS], ok[:STEPS]
    ridx, rok = index[STEPS], ok[STEPS]

    left_small = pick_cols(left_rows, own_left, blk)
    right_small = pick_rows(right_cols, ridx, blk)
    highest = lax.Precision.HIGHEST

    def ordered_for(k):
        kl = lax.dynamic_index_in_dim(lidx, k, axis=0, keepdims=False)
        kok = lax.dynamic_index_in_dim(lok, k, axis=0, keepdims=False)
        return aligned_right(right_small, kl, kok, ridx, rok, blk)

    ordered = [ordered_for(k) for k in range(STEPS)]

    held = spread_roots(left_small, coldev, rowdev, nrow, ncol)
    near, far = gather_lefts(held, yhi, nrow, ncol)
    swapped = lax.ppermute(jnp.stack([near, far]), "row", [(r, r ^ 1) for r in range(nrow)])

    mine = core == 0
    tiles = [
        jnp.where(mine, near, swapped[0]),
        jnp.where(mine, swapped[0], near),
        jnp.where(mine, far, swapped[1]),
        jnp.where(mine, swapped[1], far),
    ]
    total = None
    for k in range(STEPS):
        part = jnp.dot(tiles[k], ordered[k], precision=highest, preferred_element_type=jnp.float32)
        part = part if k == 0 else shifted(part, "col", k)
        total = part if total is None else total + part
    return total


def solution(mesh):
    return jax.shard_map(
        steps,
        mesh=mesh,
        in_specs=(P("col", "row"), P("col", "row"), P(), P()),
        out_specs=P("col", "row"),
        check_vma=False,
    )
```

```python
import jax
import jax.numpy as jnp
from jax import lax
from jax.sharding import PartitionSpec as P


STEPS = 4
CAP = 3
QUAD = 4


def slots(flags, cap):
    full = (flags != 0).astype(jnp.int32)
    width = full.shape[-1]
    where = jnp.arange(width, dtype=jnp.int32)
    before = (where[None, :] < where[:, None]).astype(jnp.int32)
    rank = jnp.sum(full[:, None, :] * before[None, :, :], axis=-1)
    hit = (full[:, None, :] == 1) & (rank[:, None, :] == jnp.arange(cap, dtype=jnp.int32)[None, :, None])
    index = jnp.sum(jnp.where(hit, where[None, None, :], 0), axis=-1)
    return index, jnp.any(hit, axis=-1)


def pick_cols(x, index, blk):
    return jnp.concatenate(
        [lax.dynamic_slice_in_dim(x, index[s] * blk, blk, axis=1) for s in range(index.shape[0])], axis=1
    )


def pick_rows(x, index, blk):
    return jnp.concatenate(
        [lax.dynamic_slice_in_dim(x, index[s] * blk, blk, axis=0) for s in range(index.shape[0])], axis=0
    )


def aligned_right(right, lidx, lok, ridx, rok, blk):
    weight = ((lidx[:, None] == ridx[None, :]) & lok[:, None] & rok[None, :]).astype(right.dtype)
    blocks = right.reshape(ridx.shape[0], blk, right.shape[1])
    picked = jnp.einsum("ij,jab->iab", weight, blocks, precision=lax.Precision.HIGHEST)
    return picked.reshape(right.shape)


def flat_pairs(moves, ncol):
    return [(sr * ncol + sc, dr * ncol + dc) for (sr, sc), (dr, dc) in moves]


def spread_roots(left_small, coldev, rowdev, nrow, ncol):
    flat = ("row", "col")
    received = []
    for hop in range(1, nrow // QUAD):
        moves = []
        for c in range(ncol):
            for k in range(STEPS):
                root = (c + k) % nrow
                moves.append(((root, c), ((root + QUAD * hop) % nrow, c)))
        received.append(lax.ppermute(left_small, flat, flat_pairs(moves, ncol)))
    held = received[0]
    for more in received[1:]:
        held = held + more
    is_root = ((rowdev - coldev) % nrow) < STEPS
    return jnp.where(is_root, left_small, held)


def gather_lefts(held, yhi, nrow, ncol):
    flat = ("row", "col")
    received = []
    for j in range(2):
        moves = []
        for q in range(ncol):
            for x in range(nrow // QUAD):
                for k in range(QUAD):
                    target = x * QUAD + ((k // 2 + j) % 2) * 2 + k % 2
                    moves.append(((x * QUAD + q % QUAD, (q - k) % ncol), (target, q)))
        received.append(lax.ppermute(held, flat, flat_pairs(moves, ncol)))
    near = jnp.where(yhi == 0, received[0], received[1])
    far = jnp.where(yhi == 0, received[1], received[0])
    return near, far


def send_home(part, near_k, to_partner, nrow, ncol):
    flat = ("row", "col")
    moves = []
    for r in range(nrow):
        for q in range(ncol):
            moves.append(((r, q), (r ^ 1 if to_partner else r, (q - r % 2 - near_k) % ncol)))
    return lax.ppermute(part, flat, flat_pairs(moves, ncol))


def steps(left_rows, right_cols, left_pattern, right_pattern):
    nrow = lax.axis_size("row")
    ncol = lax.axis_size("col")
    assert nrow == ncol and nrow % QUAD == 0 and STEPS == QUAD == 4
    _, left_width = left_rows.shape
    right_height, blk = right_cols.shape
    per_k = left_width // blk
    trows = right_height // blk
    rowdev = lax.axis_index("row")
    coldev = lax.axis_index("col")
    core = rowdev % 2
    yhi = (rowdev // 2) % 2

    own_flags = lax.dynamic_slice(left_pattern, (coldev, rowdev * per_k), (1, per_k))
    own_left = slots(own_flags, CAP)[0][0]
    grid_rows = jnp.stack([(coldev - k) % ncol for k in range(STEPS)])
    lefts = left_pattern[grid_rows[:, None], coldev * per_k + jnp.arange(per_k)[None, :]]
    own_right = lax.dynamic_slice(right_pattern, (coldev * trows, rowdev), (trows, 1)).reshape(1, trows)
    index, ok = slots(jnp.concatenate([lefts, own_right], axis=0), CAP)
    lidx, lok = index[:STEPS], ok[:STEPS]
    ridx, rok = index[STEPS], ok[STEPS]

    left_small = pick_cols(left_rows, own_left, blk)
    right_small = pick_rows(right_cols, ridx, blk)

    def ordered_for(k):
        kl = lax.dynamic_index_in_dim(lidx, k, axis=0, keepdims=False)
        kok = lax.dynamic_index_in_dim(lok, k, axis=0, keepdims=False)
        return aligned_right(right_small, kl, kok, ridx, rok, blk)

    for_partner = jnp.stack([ordered_for(1 - core), ordered_for(3 - core)])
    from_partner = lax.ppermute(for_partner, "row", [(r, r ^ 1) for r in range(nrow)])
    own_near, own_far = ordered_for(core), ordered_for(core + 2)
    plans = [(0, False, own_near), (2, False, own_far), (0, True, from_partner[0]), (2, True, from_partner[1])]

    held = spread_roots(left_small, coldev, rowdev, nrow, ncol)
    near, far = gather_lefts(held, yhi, nrow, ncol)

    total = None
    for near_k, to_partner, right in plans:
        left = near if near_k == 0 else far
        part = jnp.dot(left, right, precision=lax.Precision.HIGH, preferred_element_type=jnp.float32)
        part = send_home(part, near_k, to_partner, nrow, ncol)
        total = part if total is None else total + part
    return total


def solution(mesh):
    return jax.shard_map(
        steps,
        mesh=mesh,
        in_specs=(P("col", "row"), P("col", "row"), P(), P()),
        out_specs=P("col", "row"),
        check_vma=False,
    )
```
